512 devices in a mesh: ep: 128 (over y, z, core), dp: 4 (over x).
Axes of the slice: x: 4, y: 8, z: 8, core: 2. Of those that a mesh axis runs over, the one named last changes fastest.
Arguments:
- tokens: bfloat16 [2, 2048, 3584], P(None, ('ep', 'dp')), may hold values from -6 to 6
- routing: int32 [2, 2048, 8], P(None, 'ep'), may hold values from 0 to 127, all different within a row; in each aligned block of 16 rows (0 to 15, 16 to 31, ..., all dimensions but the last counted through in order) at most 2 rows name the same one
- gate_values: float32 [2, 2048, 8], P(None, 'ep'), may hold values from 0.05 to 0.5
- held_weight: bfloat16 [128, 3584, 1024], P('ep', None, 'dp'), may hold values from -0.09375 to 0.09375
- scale_table: float32 [128, 28, 8], P(None, None, 'dp'), may hold values from 0.25 to 4
- old_expert: int32 [128], replicated, may hold values from 0 to 127, as said below
- new_expert: int32 [128], replicated, may hold values from 0 to 127, as said below
Outputs:
- combined: bfloat16 [2, 2048, 1024], P(None, 'ep', 'dp')
- moved_weight: bfloat16 [128, 3584, 1024], P('ep', None, 'dp')
The draws below stay inside these ranges and needn't reach their ends.
Inputs may be any that keep to these rules, and one draw needn't show every extreme that they name: `routing`: each row names 8 different experts; in each aligned block of 16 token rows of a step no expert is named by more than 2 rows. `old_expert`: A permutation of the experts over the slots. `new_expert`: A permutation of the experts over the slots; it equals old_expert except at exactly 32 slots, whose experts are permuted among themselves so that each of them changes.
All inputs are finite; a program needn't handle non-finite values.
Results may differ from the reference program's by a relative error of at most 0.0039.
Values may be sent and summed in bfloat16 or wider, within the bound.
No kernel may reach another device: no remote copies, remote signals or barrier semaphores. Data moves between devices by JAX's collectives and lax.ppermute only.
A program may use at most 64 MiB of HBM per device.

```python
import math
import jax
import jax.numpy as jnp
import numpy as np
from jax import lax

D = 3584
FF = 1024
BLK = 128
TOP = 8
STEPS = 2
TOK_DEV = 4
EXPERTS = 128
TOKENS = 2048
CAP = 2
MOVED = 32
N_DP = 4


def placement_pair(key):
    base = jax.random.fold_in(key, 11)
    first_key, second_key = jax.random.split(base)
    old_expert = jax.random.permutation(first_key, EXPERTS).astype(jnp.int32)
    chosen = jax.random.permutation(second_key, EXPERTS)[:MOVED]
    new_expert = old_expert.at[chosen].set(old_expert[jnp.roll(chosen, 1)])
    return (old_expert, new_expert.astype(jnp.int32))


def draw_old_expert(key, part):
    return placement_pair(key)[0]


def draw_new_expert(key, part):
    return placement_pair(key)[1]


def level_of(key, shape, cuts, low, largest):
    factor_of, own = 1.0, jax.random.fold_in(key, 6)
    for position, blocks in cuts:
        heights = jnp.exp(jax.random.uniform(jax.random.fold_in(own, position), (blocks,), jnp.float32, low / len(cuts), largest / len(cuts)))
        factor_of = factor_of * jnp.repeat(heights, shape[position] // blocks).reshape([-1 if axis == position else 1 for axis in range(len(shape))])
    return factor_of


def routed_block(own_key, own, number, rows, count, top, bound, lean):
    sequence = jax.random.permutation(own_key, count)
    heavy_load, common = shares(count, rows * top, bound, lean, True), shares(count, rows * top, bound, lean, False)
    places = jnp.arange(count)

    def named(lengths, offset_by):
        used = int((lengths > 0).sum())
        fixed = max(1, used // 4)
        moved = fixed + (places - fixed + offset_by * (used - fixed)) % max(1, count - fixed)
        return jnp.zeros((count,), jnp.int32).at[sequence[jnp.where(places < fixed, places, moved)]].set(jnp.asarray(lengths, jnp.int32))

    lengths = jnp.where(number % 4 == 0, named(heavy_load, number // 4), named(common, number - number // 4 - 1))
    mixed = jax.random.permutation(jax.random.fold_in(own, 3), count)
    source_of, taker = mixed[0:count // 2 * 2:2], mixed[1:count // 2 * 2:2]
    room = jnp.minimum(lengths[source_of] - 1, bound - lengths[taker]) // 2
    room = jnp.where((source_of == sequence[0]) | (taker == sequence[0]) | (lengths[taker] == 0), 0, jnp.maximum(room, 0))
    moved = jax.random.randint(jax.random.fold_in(own, 4), (count // 2,), 0, 1 << 20) % (room + 1)
    lengths = lengths.at[source_of].add(-moved).at[taker].add(moved)
    members = jnp.searchsorted(jnp.cumsum(lengths), jnp.arange(rows * top), side="right").astype(jnp.int32)
    grid = members.reshape(top, rows).T
    grid = grid[jax.random.permutation(jax.random.fold_in(own, 1), rows)]
    offset_by = jax.random.randint(jax.random.fold_in(own, 2), (rows, 1), 0, top)
    return jnp.take_along_axis(grid, (jnp.arange(top)[None, :] + offset_by) % top, axis=1)


def shares(amount, total, limit, slope, full):
    weights = [(1 << 20) // math.isqrt(rank ** slope) + 1 for rank in range(1, amount + 1)]
    largest = limit if full else min(limit, max(-(-total // amount), total * weights[0] // sum(weights)))
    least = 1 if total - largest >= amount - 1 else 0
    given, surplus = [largest] + [least] * (amount - 1), total - largest - least * (amount - 1)
    while surplus > 0:
        candidates = [i for i in range(1, amount) if given[i] < largest] or [i for i in range(1, amount) if given[i] < limit]
        whole, left = sum([weights[i] for i in candidates]), surplus
        for i in candidates:
            addition = min(limit - given[i], max(1, left * weights[i] // whole), surplus)
            given[i] = given[i] + addition
            surplus = surplus - addition
    return np.array(given)


def scatter_about(stream_key, dims, spread, bound, pieces=(), kind=jnp.bfloat16):
    array = spread * jax.random.normal(stream_key, dims, jnp.float32)
    if pieces:
        array = array * level_of(stream_key, dims, pieces, -0.22, 0.18)
    return jnp.clip(array, -bound, bound).astype(kind)


def setup_inputs(seed: int = 0) -> dict:
    keys = jax.random.split(jax.random.key(seed), 8)
    tokens = scatter_about(keys[0], (STEPS, TOKENS, D), 1.0, 6.0, ((1, 512),))
    routing_keys = jax.random.split(jax.random.fold_in(keys[1], 1), STEPS * TOKENS // (N_DP * TOK_DEV))
    routing_turns = jax.random.permutation(jax.random.fold_in(keys[1], 3), STEPS * TOKENS // (N_DP * TOK_DEV))
    routing = jax.vmap(lambda own, number: routed_block(jax.random.fold_in(keys[1], 2), own, number, N_DP * TOK_DEV, EXPERTS, TOP, CAP, 2))(routing_keys, routing_turns).reshape((STEPS, TOKENS, TOP))
    gate_values = jnp.clip(0.05 + 0.45 * jax.random.uniform(keys[2], (STEPS, TOKENS, TOP), jnp.float32) ** level_of(keys[2], (STEPS, TOKENS, TOP), ((1, 128),), -0.2, 0.2), 0.05, 0.5)
    held_weight = scatter_about(keys[3], (EXPERTS, D, FF), D ** -0.5, 0.09375, ((0, 128), (2, 4)))
    scale_table = jnp.clip(jnp.exp(math.log(4.0) - 2.7725887 * jax.random.uniform(keys[4], (EXPERTS, D // BLK, FF // BLK), jnp.float32) ** level_of(keys[4], (EXPERTS, D // BLK, FF // BLK), ((2, 4),), -0.2, 0.2)), 0.25, 4.0)
    old_expert = draw_old_expert(jax.random.fold_in(keys[7], 71), 0)
    new_expert = draw_new_expert(jax.random.fold_in(keys[7], 71), 0)
    return {"tokens": tokens, "routing": routing, "gate_values": gate_values, "held_weight": held_weight, "scale_table": scale_table, "old_expert": old_expert, "new_expert": new_expert}


def inverse_place(expert_at):
    count = expert_at.shape[0]
    labels = jnp.arange(count, dtype=jnp.int32)
    match = expert_at[None, :] == labels[:, None]
    return jnp.sum(jnp.where(match, labels[None, :], 0), axis=1).astype(jnp.int32)


def dequantized(weight_block, scales):
    widened = jnp.repeat(jnp.repeat(scales, BLK, axis=0), BLK, axis=1)
    return weight_block.astype(jnp.float32) * widened


def decode_once(token_rows, routing, gate_values, held_weight, owners, scale_table):
    group_size = N_DP * TOK_DEV
    group_count = TOKENS // group_size
    pair_ids = routing.reshape(-1).astype(jnp.int32)
    pair_total = pair_ids.shape[0]
    labels = jnp.arange(EXPERTS, dtype=jnp.int32)
    onehot = (pair_ids[:, None] == labels[None, :]).astype(jnp.int32)
    onehot = onehot.reshape(group_count, group_size * TOP, EXPERTS)
    before = jnp.cumsum(onehot, axis=1) - onehot
    slot_rank = jnp.sum(before * onehot, axis=2).reshape(-1).astype(jnp.int32)
    pair_index = jnp.arange(pair_total, dtype=jnp.int32)
    group_index = (pair_index // (group_size * TOP)).astype(jnp.int32)
    slot_table = jnp.full((EXPERTS, group_count, CAP), -1, jnp.int32)
    slot_table = slot_table.at[pair_ids, group_index, slot_rank].set(pair_index)
    flat_gates = gate_values.reshape(-1)

    def visit_expert(combined, expert):
        slot_pairs = slot_table[expert].reshape(-1)
        live_slot = slot_pairs >= 0
        safe_slot = jnp.where(live_slot, slot_pairs, 0).astype(jnp.int32)
        token_index = (safe_slot // TOP).astype(jnp.int32)
        features = token_rows[token_index].astype(jnp.float32)
        weights = dequantized(held_weight[owners[expert]], scale_table[expert])
        hidden = jnp.dot(features, weights, precision=lax.Precision.HIGHEST, preferred_element_type=jnp.float32)
        rounded = lax.optimization_barrier(jax.nn.silu(hidden).astype(jnp.bfloat16))
        activated = rounded.astype(jnp.float32)
        weighted = jnp.where(live_slot[:, None], flat_gates[safe_slot][:, None] * activated, jnp.float32(0.0))
        return combined.at[token_index].add(weighted), None

    start = jnp.zeros((TOKENS, FF), jnp.float32)
    combined, _ = lax.scan(visit_expert, start, jnp.arange(EXPERTS, dtype=jnp.int32))
    return combined


def reference(tokens, routing, gate_values, held_weight, scale_table, old_expert, new_expert):
    owners = inverse_place(old_expert)
    moved_weight = held_weight[owners[new_expert]]
    results = []
    for decode_step in range(STEPS):
        results.append(decode_once(tokens[decode_step], routing[decode_step], gate_values[decode_step], held_weight, owners, scale_table))
    return jnp.stack(results).astype(jnp.bfloat16), moved_weight
```

```python
import jax
import jax.numpy as jnp
from jax import lax
from jax.sharding import PartitionSpec as P


def inverse_place(expert_at):
    count = expert_at.shape[0]
    labels = jnp.arange(count, dtype=jnp.int32)
    match = expert_at[None, :] == labels[:, None]
    return jnp.sum(jnp.where(match, labels[None, :], 0), axis=1)


def source_slots(old_expert, new_expert):
    labels = jnp.arange(old_expert.shape[0], dtype=jnp.int32)
    match = old_expert[None, :] == new_expert[:, None]
    return jnp.sum(jnp.where(match, labels[None, :], 0), axis=1)


def route_targets(routing, owners, peers, capacity):
    steps, group_size, top_count = routing.shape
    labels = jnp.arange(peers, dtype=jnp.int32)
    pair_ids = routing.reshape(steps, group_size * top_count)
    onehot = (pair_ids[:, :, None] == labels[None, None, :]).astype(jnp.int32)
    before = jnp.cumsum(onehot, axis=1) - onehot
    rank = jnp.sum(before * onehot, axis=2)
    slot = owners[pair_ids]
    step = jnp.arange(steps, dtype=jnp.int32)[:, None]
    return (slot * steps + step) * capacity + rank


def shards(tokens, routing, gate_values, held_weight, scale_table, old_expert, new_expert):
    peers = lax.axis_size("ep")
    n_dp = lax.axis_size("dp")
    my_slot = lax.axis_index("ep")
    my_dp = lax.axis_index("dp")
    steps, group_size, top_count = routing.shape
    capacity = 2
    old_block = held_weight[0]
    rows, cols = old_block.shape
    row_part = rows // n_dp
    blk = rows // scale_table.shape[1]
    owners = inverse_place(old_expert)
    sources = source_slots(old_expert, new_expert)

    w_rows = lax.all_to_all(old_block, "dp", split_axis=0, concat_axis=1, tiled=True)
    my_scales = lax.all_gather(scale_table[old_expert[my_slot]], "dp", axis=1, tiled=True)
    row_blocks = row_part // blk
    my_scales = lax.dynamic_slice_in_dim(my_scales, my_dp * row_blocks, row_blocks, axis=0)
    widened = jnp.repeat(jnp.repeat(my_scales, blk, axis=0), blk, axis=1)
    w32 = w_rows.astype(jnp.float32) * widened
    w_hi = w32.astype(jnp.bfloat16)
    w_lo = (w32 - w_hi.astype(jnp.float32)).astype(jnp.bfloat16)

    feats = lax.all_to_all(tokens, "dp", split_axis=2, concat_axis=1, tiled=True)

    target = route_targets(routing, owners, peers, capacity)
    token_of = jnp.broadcast_to(
        jnp.arange(group_size, dtype=jnp.int32)[None, :, None], (steps, group_size, top_count)
    ).reshape(steps, -1)
    step_of = jnp.broadcast_to(jnp.arange(steps, dtype=jnp.int32)[:, None], token_of.shape)
    pick = jnp.zeros((peers * steps * capacity,), jnp.int32).at[target.reshape(-1)].set(
        (step_of * group_size + token_of).reshape(-1)
    )
    send_tokens = feats.reshape(steps * group_size, row_part)[pick]
    send_tokens = send_tokens.reshape(peers, steps * capacity * row_part)

    pieces = old_block.reshape(peers, (rows // peers) * cols)
    first = lax.all_to_all(
        jnp.concatenate([pieces, send_tokens], axis=1), "ep", split_axis=0, concat_axis=0, tiled=True
    )
    piece_len = pieces.shape[1]
    gathered_pieces = jnp.take(first[:, :piece_len], sources, axis=0)
    arrived = first[:, piece_len:].reshape(peers * steps * capacity, row_part)

    partial = jnp.dot(arrived, w_hi, preferred_element_type=jnp.float32) + jnp.dot(
        arrived, w_lo, preferred_element_type=jnp.float32
    )
    hidden = lax.psum_scatter(partial, "dp", scatter_dimension=1, tiled=True)
    act = jax.nn.silu(hidden).astype(jnp.bfloat16)
    act = act.reshape(peers, steps * capacity * act.shape[1])

    second = lax.all_to_all(
        jnp.concatenate([gathered_pieces, act], axis=1), "ep", split_axis=0, concat_axis=0, tiled=True
    )
    new_block = second[:, :piece_len].reshape(rows, cols)
    returned = second[:, piece_len:].reshape(peers * steps * capacity, -1)
    picked = returned[target].astype(jnp.float32).reshape(steps, group_size, top_count, -1)
    combined = jnp.sum(gate_values[:, :, :, None] * picked, axis=2).astype(jnp.bfloat16)
    return (combined, new_block[None])


def solution(mesh):
    placed = (
        P(None, ("ep", "dp"), None),
        P(None, "ep", None),
        P(None, "ep", None),
        P("ep", None, "dp"),
        P(None, None, "dp"),
        P(),
        P(),
    )
    return jax.shard_map(
        shards,
        mesh=mesh,
        in_specs=placed,
        out_specs=(P(None, "ep", "dp"), P("ep", None, "dp")),
        check_vma=False,
    )
```

```python
import jax
import jax.numpy as jnp
from jax import lax
from jax.sharding import PartitionSpec as P


def inverse_place(expert_at):
    count = expert_at.shape[0]
    labels = jnp.arange(count, dtype=jnp.int32)
    match = expert_at[None, :] == labels[:, None]
    return jnp.sum(jnp.where(match, labels[None, :], 0), axis=1)


def source_slots(old_expert, new_expert):
    labels = jnp.arange(old_expert.shape[0], dtype=jnp.int32)
    match = old_expert[None, :] == new_expert[:, None]
    return jnp.sum(jnp.where(match, labels[None, :], 0), axis=1)


def route_targets(routing, owners, peers, capacity):
    steps, group_size, top_count = routing.shape
    labels = jnp.arange(peers, dtype=jnp.int32)
    pair_ids = routing.reshape(steps, group_size * top_count)
    onehot = (pair_ids[:, :, None] == labels[None, None, :]).astype(jnp.int32)
    before = jnp.cumsum(onehot, axis=1) - onehot
    rank = jnp.sum(before * onehot, axis=2)
    slot = owners[pair_ids]
    step = jnp.arange(steps, dtype=jnp.int32)[:, None]
    return (slot * steps + step) * capacity + rank


def dp_exchange(parts, n_dp, my_dp):
    got = [parts[my_dp]]
    for shift in range(1, n_dp):
        pairs = [(k, (k + shift) % n_dp) for k in range(n_dp)]
        got.append(lax.ppermute(parts[(my_dp + shift) % n_dp], "dp", pairs))
    by_shift = jnp.stack(got)
    order = (my_dp - jnp.arange(n_dp, dtype=jnp.int32)) % n_dp
    return by_shift[order]


def shards(tokens, routing, gate_values, held_weight, scale_table, old_expert, new_expert):
    peers = lax.axis_size("ep")
    n_dp = lax.axis_size("dp")
    my_slot = lax.axis_index("ep")
    my_dp = lax.axis_index("dp")
    steps, group_size, top_count = routing.shape
    capacity = 2
    old_block = held_weight[0]
    rows, cols = old_block.shape
    row_part = rows // n_dp
    blk = rows // scale_table.shape[1]
    owners = inverse_place(old_expert)
    sources = source_slots(old_expert, new_expert)

    pieces = old_block.reshape(peers, rows // peers, cols)
    staged = lax.all_to_all(pieces, "ep", split_axis=0, concat_axis=0, tiled=True)

    w_parts = dp_exchange(old_block.reshape(n_dp, row_part, cols), n_dp, my_dp)
    w_rows = jnp.transpose(w_parts, (1, 0, 2)).reshape(row_part, n_dp * cols)
    own_scales = scale_table[old_expert[my_slot]]
    row_blocks = row_part // blk
    s_parts = dp_exchange(own_scales.reshape(n_dp, row_blocks, own_scales.shape[1]), n_dp, my_dp)
    my_scales = jnp.transpose(s_parts, (1, 0, 2)).reshape(row_blocks, -1)
    widened = jnp.repeat(jnp.repeat(my_scales, blk, axis=0), blk, axis=1)
    w32 = w_rows.astype(jnp.float32) * widened
    hi32 = lax.reduce_precision(w32, exponent_bits=8, mantissa_bits=7)
    w_hi = hi32.astype(jnp.bfloat16)
    w_lo = (w32 - hi32).astype(jnp.bfloat16)

    t_parts = dp_exchange(
        jnp.transpose(tokens.reshape(steps, tokens.shape[1], n_dp, row_part), (2, 0, 1, 3)), n_dp, my_dp
    )
    feats = jnp.transpose(t_parts, (1, 0, 2, 3)).reshape(steps * group_size, row_part)

    target = route_targets(routing, owners, peers, capacity)
    token_of = jnp.broadcast_to(
        jnp.arange(group_size, dtype=jnp.int32)[None, :, None], (steps, group_size, top_count)
    ).reshape(steps, -1)
    step_of = jnp.broadcast_to(jnp.arange(steps, dtype=jnp.int32)[:, None], token_of.shape)
    pick = jnp.zeros((peers * steps * capacity,), jnp.int32).at[target.reshape(-1)].set(
        (step_of * group_size + token_of).reshape(-1)
    )
    send_tokens = feats[pick].reshape(peers, steps * capacity, row_part)
    arrived = lax.all_to_all(send_tokens, "ep", split_axis=0, concat_axis=0, tiled=True)

    new_block = lax.all_to_all(
        jnp.take(staged, sources, axis=0), "ep", split_axis=0, concat_axis=0, tiled=True
    ).reshape(rows, cols)

    arrived = arrived.reshape(peers * steps * capacity, row_part)
    partial = jnp.dot(arrived, w_hi, preferred_element_type=jnp.float32) + jnp.dot(
        arrived, w_lo, preferred_element_type=jnp.float32
    )
    hidden = lax.psum_scatter(partial, "dp", scatter_dimension=1, tiled=True)
    act = jax.nn.silu(hidden).astype(jnp.bfloat16)
    act = act.reshape(peers, steps * capacity, act.shape[1])
    returned = lax.all_to_all(act, "ep", split_axis=0, concat_axis=0, tiled=True)
    returned = returned.reshape(peers * steps * capacity, -1)
    picked = returned[target].astype(jnp.float32).reshape(steps, group_size, top_count, -1)
    combined = jnp.sum(gate_values[:, :, :, None] * picked, axis=2).astype(jnp.bfloat16)
    return (combined, new_block[None])


def solution(mesh):
    placed = (
        P(None, ("ep", "dp"), None),
        P(None, "ep", None),
        P(None, "ep", None),
        P("ep", None, "dp"),
        P(None, None, "dp"),
        P(),
        P(),
    )
    return jax.shard_map(
        shards,
        mesh=mesh,
        in_specs=placed,
        out_specs=(P(None, "ep", "dp"), P("ep", None, "dp")),
        check_vma=False,
    )
```

```python
import jax
import jax.numpy as jnp
from jax import lax
from jax.sharding import PartitionSpec as P


def inverse_place(expert_at):
    count = expert_at.shape[0]
    labels = jnp.arange(count, dtype=jnp.int32)
    match = expert_at[None, :] == labels[:, None]
    return jnp.sum(jnp.where(match, labels[None, :], 0), axis=1)


def source_slots(old_expert, new_expert):
    labels = jnp.arange(old_expert.shape[0], dtype=jnp.int32)
    match = old_expert[None, :] == new_expert[:, None]
    return jnp.sum(jnp.where(match, labels[None, :], 0), axis=1)


def route_targets(routing, owners, peers, capacity):
    steps, group_size, top_count = routing.shape
    labels = jnp.arange(peers, dtype=jnp.int32)
    pair_ids = routing.reshape(steps, group_size * top_count)
    onehot = (pair_ids[:, :, None] == labels[None, None, :]).astype(jnp.int32)
    before = jnp.cumsum(onehot, axis=1) - onehot
    rank = jnp.sum(before * onehot, axis=2)
    slot = owners[pair_ids]
    step = jnp.arange(steps, dtype=jnp.int32)[:, None]
    return (slot * steps + step) * capacity + rank


def dp_shifts(parts, n_dp, my_dp):
    got = [parts[my_dp]]
    for shift in range(1, n_dp):
        pairs = [(k, (k + shift) % n_dp) for k in range(n_dp)]
        got.append(lax.ppermute(parts[(my_dp + shift) % n_dp], "dp", pairs))
    return got


def shards(tokens, routing, gate_values, held_weight, scale_table, old_expert, new_expert):
    peers = lax.axis_size("ep")
    n_dp = lax.axis_size("dp")
    my_slot = lax.axis_index("ep")
    my_dp = lax.axis_index("dp")
    steps, group_size, top_count = routing.shape
    local_tokens = tokens.shape[1]
    capacity = 2
    old_block = held_weight[0]
    rows, cols = old_block.shape
    row_part = rows // n_dp
    blk = rows // scale_table.shape[1]
    owners = inverse_place(old_expert)
    sources = source_slots(old_expert, new_expert)

    pieces = old_block.reshape(peers, rows // peers, cols)
    staged = lax.all_to_all(pieces, "ep", split_axis=0, concat_axis=0, tiled=True)

    w_parts = dp_shifts(old_block.reshape(n_dp, row_part, cols), n_dp, my_dp)
    own_scales = scale_table[old_expert[my_slot]]
    row_blocks = row_part // blk
    s_parts = dp_shifts(own_scales.reshape(n_dp, row_blocks, own_scales.shape[1]), n_dp, my_dp)
    w_rows = jnp.concatenate(w_parts, axis=1)
    my_scales = jnp.concatenate(s_parts, axis=1)
    widened = jnp.repeat(jnp.repeat(my_scales, blk, axis=0), blk, axis=1)
    w32 = w_rows.astype(jnp.float32) * widened
    hi32 = lax.reduce_precision(w32, exponent_bits=8, mantissa_bits=7)
    w_hi = hi32.astype(jnp.bfloat16)
    w_lo = (w32 - hi32).astype(jnp.bfloat16)

    t_parts = dp_shifts(
        jnp.transpose(tokens.reshape(steps, local_tokens, n_dp, row_part), (2, 0, 1, 3)), n_dp, my_dp
    )
    feats = jnp.stack(t_parts).reshape(n_dp * steps * local_tokens, row_part)

    target = route_targets(routing, owners, peers, capacity)
    token_of = jnp.broadcast_to(
        jnp.arange(group_size, dtype=jnp.int32)[None, :, None], (steps, group_size, top_count)
    ).reshape(steps, -1)
    step_of = jnp.broadcast_to(jnp.arange(steps, dtype=jnp.int32)[:, None], token_of.shape)
    part_of = (my_dp - token_of // local_tokens) % n_dp
    row_of = (part_of * steps + step_of) * local_tokens + token_of % local_tokens
    pick = jnp.zeros((peers * steps * capacity,), jnp.int32).at[target.reshape(-1)].set(row_of.reshape(-1))
    send_tokens = feats[pick].reshape(peers, steps * capacity, row_part)
    staged, send_tokens = lax.optimization_barrier((staged, send_tokens))
    arrived = lax.all_to_all(send_tokens, "ep", split_axis=0, concat_axis=0, tiled=True)

    regrouped, arrived = lax.optimization_barrier((jnp.take(staged, sources, axis=0), arrived))
    new_block = lax.all_to_all(regrouped, "ep", split_axis=0, concat_axis=0, tiled=True).reshape(rows, cols)

    arrived = arrived.reshape(peers * steps * capacity, row_part)
    partial = jnp.dot(arrived, w_hi, preferred_element_type=jnp.float32) + jnp.dot(
        arrived, w_lo, preferred_element_type=jnp.float32
    )
    hidden = partial[:, :cols]
    for shift in range(1, n_dp):
        pairs = [(k, (k - shift) % n_dp) for k in range(n_dp)]
        hidden = hidden + lax.ppermute(partial[:, shift * cols:(shift + 1) * cols], "dp", pairs)
    act = jax.nn.silu(hidden).astype(jnp.bfloat16)
    act = act.reshape(peers, steps * capacity, cols)
    act, new_block = lax.optimization_barrier((act, new_block))
    returned = lax.all_to_all(act, "ep", split_axis=0, concat_axis=0, tiled=True)
    returned = returned.reshape(peers * steps * capacity, -1)
    picked = returned[target].astype(jnp.float32).reshape(steps, group_size, top_count, -1)
    combined = jnp.sum(gate_values[:, :, :, None] * picked, axis=2).astype(jnp.bfloat16)
    return (combined, new_block[None])


def solution(mesh):
    placed = (
        P(None, ("ep", "dp"), None),
        P(None, "ep", None),
        P(None, "ep", None),
        P("ep", None, "dp"),
        P(None, None, "dp"),
        P(),
        P(),
    )
    return jax.shard_map(
        shards,
        mesh=mesh,
        in_specs=placed,
        out_specs=(P(None, "ep", "dp"), P("ep", None, "dp")),
        check_vma=False,
    )
```

```python
import jax
import jax.numpy as jnp
from jax import lax
from jax.sharding import PartitionSpec as P


def inverse_place(expert_at):
    count = expert_at.shape[0]
    labels = jnp.arange(count, dtype=jnp.int32)
    match = expert_at[None, :] == labels[:, None]
    return jnp.sum(jnp.where(match, labels[None, :], 0), axis=1)


def source_slots(old_expert, new_expert):
    labels = jnp.arange(old_expert.shape[0], dtype=jnp.int32)
    match = old_expert[None, :] == new_expert[:, None]
    return jnp.sum(jnp.where(match, labels[None, :], 0), axis=1)


def route_targets(routing, owners, peers, capacity):
    steps, group_size, top_count = routing.shape
    labels = jnp.arange(peers, dtype=jnp.int32)
    pair_ids = routing.reshape(steps, group_size * top_count)
    onehot = (pair_ids[:, :, None] == labels[None, None, :]).astype(jnp.int32)
    before = jnp.cumsum(onehot, axis=1) - onehot
    rank = jnp.sum(before * onehot, axis=2)
    slot = owners[pair_ids]
    step = jnp.arange(steps, dtype=jnp.int32)[:, None]
    return (slot * steps + step) * capacity + rank


def dp_shifts(parts, n_dp, my_dp):
    got = [parts[my_dp]]
    for shift in range(1, n_dp):
        pairs = [(k, (k + shift) % n_dp) for k in range(n_dp)]
        got.append(lax.ppermute(parts[(my_dp + shift) % n_dp], "dp", pairs))
    return got


def shards(tokens, routing, gate_values, held_weight, scale_table, old_expert, new_expert):
    peers = lax.axis_size("ep")
    n_dp = lax.axis_size("dp")
    my_slot = lax.axis_index("ep")
    my_dp = lax.axis_index("dp")
    steps, group_size, top_count = routing.shape
    local_tokens = tokens.shape[1]
    capacity = 2
    old_block = held_weight[0]
    rows, cols = old_block.shape
    row_part = rows // n_dp
    blk = rows // scale_table.shape[1]
    owners = inverse_place(old_expert)
    sources = source_slots(old_expert, new_expert)

    pieces = old_block.reshape(peers, rows // peers, cols)
    staged = lax.all_to_all(pieces, "ep", split_axis=0, concat_axis=0, tiled=True)

    own_scales = scale_table[old_expert[my_slot]]
    widened = jnp.repeat(jnp.repeat(own_scales, blk, axis=0), blk, axis=1)
    w32 = old_block.astype(jnp.float32) * widened
    hi32 = lax.reduce_precision(w32, exponent_bits=8, mantissa_bits=7)
    w_pair = jnp.stack([hi32.astype(jnp.bfloat16), (w32 - hi32).astype(jnp.bfloat16)])
    w_out = jnp.transpose(w_pair.reshape(2, n_dp, row_part, cols), (1, 0, 2, 3))
    t_out = jnp.transpose(tokens.reshape(steps, local_tokens, n_dp, row_part), (2, 0, 1, 3))
    token_rows = steps * local_tokens * row_part // cols
    payload = jnp.concatenate(
        [t_out.reshape(n_dp, token_rows, cols), w_out.reshape(n_dp, 2 * row_part, cols)], axis=1
    )
    got = dp_shifts(payload, n_dp, my_dp)
    feats = jnp.stack([g[:token_rows] for g in got]).reshape(n_dp * steps * local_tokens, row_part)
    w_got = [g[token_rows:].reshape(2, row_part, cols) for g in got]
    w_hi = jnp.concatenate([w[0] for w in w_got], axis=1)
    w_lo = jnp.concatenate([w[1] for w in w_got], axis=1)

    target = route_targets(routing, owners, peers, capacity)
    token_of = jnp.broadcast_to(
        jnp.arange(group_size, dtype=jnp.int32)[None, :, None], (steps, group_size, top_count)
    ).reshape(steps, -1)
    step_of = jnp.broadcast_to(jnp.arange(steps, dtype=jnp.int32)[:, None], token_of.shape)
    part_of = (my_dp - token_of // local_tokens) % n_dp
    row_of = (part_of * steps + step_of) * local_tokens + token_of % local_tokens
    pick = jnp.zeros((peers * steps * capacity,), jnp.int32).at[target.reshape(-1)].set(row_of.reshape(-1))
    send_tokens = feats[pick].reshape(peers, steps * capacity, row_part)
    staged, send_tokens, w_hi, w_lo = lax.optimization_barrier((staged, send_tokens, w_hi, w_lo))
    arrived = lax.all_to_all(send_tokens, "ep", split_axis=0, concat_axis=0, tiled=True)

    regrouped, arrived = lax.optimization_barrier((jnp.take(staged, sources, axis=0), arrived))
    new_block = lax.all_to_all(regrouped, "ep", split_axis=0, concat_axis=0, tiled=True).reshape(rows, cols)

    arrived = arrived.reshape(peers * steps * capacity, row_part)
    partial = jnp.dot(arrived, w_hi, preferred_element_type=jnp.float32) + jnp.dot(
        arrived, w_lo, preferred_element_type=jnp.float32
    )
    hidden = partial[:, :cols]
    for shift in range(1, n_dp):
        pairs = [(k, (k - shift) % n_dp) for k in range(n_dp)]
        hidden = hidden + lax.ppermute(partial[:, shift * cols:(shift + 1) * cols], "dp", pairs)
    act = jax.nn.silu(hidden).astype(jnp.bfloat16)
    act = act.reshape(peers, steps * capacity, cols)
    act, new_block = lax.optimization_barrier((act, new_block))
    returned = lax.all_to_all(act, "ep", split_axis=0, concat_axis=0, tiled=True)
    returned = returned.reshape(peers * steps * capacity, -1)
    picked = returned[target].astype(jnp.float32).reshape(steps, group_size, top_count, -1)
    combined = jnp.sum(gate_values[:, :, :, None] * picked, axis=2).astype(jnp.bfloat16)
    return (combined, new_block[None])


def solution(mesh):
    placed = (
        P(None, ("ep", "dp"), None),
        P(None, "ep", None),
        P(None, "ep", None),
        P("ep", None, "dp"),
        P(None, None, "dp"),
        P(),
        P(),
    )
    return jax.shard_map(
        shards,
        mesh=mesh,
        in_specs=placed,
        out_specs=(P(None, "ep", "dp"), P("ep", None, "dp")),
        check_vma=False,
    )
```

```python
import jax
import jax.numpy as jnp
from jax import lax
from jax.sharding import PartitionSpec as P


def inverse_place(expert_at):
    count = expert_at.shape[0]
    labels = jnp.arange(count, dtype=jnp.int32)
    match = expert_at[None, :] == labels[:, None]
    return jnp.sum(jnp.where(match, labels[None, :], 0), axis=1)


def source_slots(old_expert, new_expert):
    labels = jnp.arange(old_expert.shape[0], dtype=jnp.int32)
    match = old_expert[None, :] == new_expert[:, None]
    return jnp.sum(jnp.where(match, labels[None, :], 0), axis=1)


def route_targets(routing, owners, peers, capacity):
    steps, group_size, top_count = routing.shape
    labels = jnp.arange(peers, dtype=jnp.int32)
    pair_ids = routing.reshape(steps, group_size * top_count)
    onehot = (pair_ids[:, :, None] == labels[None, None, :]).astype(jnp.int32)
    before = jnp.cumsum(onehot, axis=1) - onehot
    rank = jnp.sum(before * onehot, axis=2)
    slot = owners[pair_ids]
    step = jnp.arange(steps, dtype=jnp.int32)[:, None]
    return (slot * steps + step) * capacity + rank


def dp_shifts(parts, n_dp, my_dp):
    got = [parts[my_dp]]
    for shift in range(1, n_dp):
        pairs = [(k, (k + shift) % n_dp) for k in range(n_dp)]
        got.append(lax.ppermute(parts[(my_dp + shift) % n_dp], "dp", pairs))
    return got


def layer(tokens, routing, gate_values, held_weight, scale_table, old_expert, new_expert):
    peers = lax.axis_size("ep")
    n_dp = lax.axis_size("dp")
    my_slot = lax.axis_index("ep")
    my_dp = lax.axis_index("dp")
    steps, group_size, top_count = routing.shape
    local_tokens = tokens.shape[1]
    capacity = 2
    old_block = held_weight[0]
    rows, cols = old_block.shape
    row_part = rows // n_dp
    blk = rows // scale_table.shape[1]
    owners = inverse_place(old_expert)
    sources = source_slots(old_expert, new_expert)

    pieces = old_block.reshape(peers, rows // peers, cols)
    staged = lax.all_to_all(pieces, "ep", split_axis=0, concat_axis=0, tiled=True)

    own_scales = scale_table[old_expert[my_slot]]
    col_scales = jnp.repeat(own_scales, blk, axis=1)
    w32 = old_block.reshape(-1, blk, cols).astype(jnp.float32) * col_scales[:, None, :]
    hi32 = lax.reduce_precision(w32, exponent_bits=8, mantissa_bits=7)
    w_hi = hi32.astype(jnp.bfloat16).reshape(rows, cols)
    w_lo = (w32 - hi32).astype(jnp.bfloat16).reshape(rows, cols)
    got = dp_shifts(
        jnp.transpose(tokens.reshape(steps, local_tokens, n_dp, row_part), (2, 0, 1, 3)), n_dp, my_dp
    )
    feats = jnp.stack(got).reshape(n_dp * steps * local_tokens, row_part)

    target = route_targets(routing, owners, peers, capacity)
    token_of = jnp.broadcast_to(
        jnp.arange(group_size, dtype=jnp.int32)[None, :, None], (steps, group_size, top_count)
    ).reshape(steps, -1)
    step_of = jnp.broadcast_to(jnp.arange(steps, dtype=jnp.int32)[:, None], token_of.shape)
    part_of = (my_dp - token_of // local_tokens) % n_dp
    row_of = (part_of * steps + step_of) * local_tokens + token_of % local_tokens
    pick = jnp.zeros((peers * steps * capacity,), jnp.int32).at[target.reshape(-1)].set(row_of.reshape(-1))
    send_tokens = feats[pick].reshape(peers, steps * capacity, row_part)
    staged, send_tokens, w_hi, w_lo = lax.optimization_barrier((staged, send_tokens, w_hi, w_lo))
    arrived = lax.all_to_all(send_tokens, "ep", split_axis=0, concat_axis=0, tiled=True)

    regrouped, arrived = lax.optimization_barrier((jnp.take(staged, sources, axis=0), arrived))
    new_block = lax.all_to_all(regrouped, "ep", split_axis=0, concat_axis=0, tiled=True).reshape(rows, cols)

    arrived = arrived.reshape(peers * steps * capacity, row_part)
    full = lax.all_gather(arrived, "dp", axis=1, tiled=True)
    hidden = jnp.dot(full, w_hi, preferred_element_type=jnp.float32) + jnp.dot(
        full, w_lo, preferred_element_type=jnp.float32
    )
    act = jax.nn.silu(hidden).astype(jnp.bfloat16)
    act = act.reshape(peers, steps * capacity, cols)
    act, new_block = lax.optimization_barrier((act, new_block))
    returned = lax.all_to_all(act, "ep", split_axis=0, concat_axis=0, tiled=True)
    returned = returned.reshape(peers * steps * capacity, -1)
    picked = returned[target].astype(jnp.float32).reshape(steps, group_size, top_count, -1)
    combined = jnp.sum(gate_values[:, :, :, None] * picked, axis=2).astype(jnp.bfloat16)
    return (combined, new_block[None])


def solution(mesh):
    placed = (
        P(None, ("ep", "dp"), None),
        P(None, "ep", None),
        P(None, "ep", None),
        P("ep", None, "dp"),
        P(None, None, "dp"),
        P(),
        P(),
    )
    return jax.shard_map(
        layer,
        mesh=mesh,
        in_specs=placed,
        out_specs=(P(None, "ep", "dp"), P("ep", None, "dp")),
        check_vma=False,
    )
```

```python
import jax
import jax.numpy as jnp
from jax import lax
from jax.sharding import PartitionSpec as P


def inverse_place(expert_at):
    count = expert_at.shape[0]
    labels = jnp.arange(count, dtype=jnp.int32)
    match = expert_at[None, :] == labels[:, None]
    return jnp.sum(jnp.where(match, labels[None, :], 0), axis=1)


def source_slots(old_expert, new_expert):
    labels = jnp.arange(old_expert.shape[0], dtype=jnp.int32)
    match = old_expert[None, :] == new_expert[:, None]
    return jnp.sum(jnp.where(match, labels[None, :], 0), axis=1)


def route_targets(routing, owners, peers, capacity):
    steps, group_size, top_count = routing.shape
    labels = jnp.arange(peers, dtype=jnp.int32)
    pair_ids = routing.reshape(steps, group_size * top_count)
    onehot = (pair_ids[:, :, None] == labels[None, None, :]).astype(jnp.int32)
    before = jnp.cumsum(onehot, axis=1) - onehot
    rank = jnp.sum(before * onehot, axis=2)
    slot = owners[pair_ids]
    step = jnp.arange(steps, dtype=jnp.int32)[:, None]
    return (slot * steps + step) * capacity + rank


def dp_shifts(parts, n_dp, my_dp):
    got = [parts[my_dp]]
    for shift in range(1, n_dp):
        pairs = [(k, (k + shift) % n_dp) for k in range(n_dp)]
        got.append(lax.ppermute(parts[(my_dp + shift) % n_dp], "dp", pairs))
    return got


def layer(tokens, routing, gate_values, held_weight, scale_table, old_expert, new_expert):
    peers = lax.axis_size("ep")
    n_dp = lax.axis_size("dp")
    my_slot = lax.axis_index("ep")
    my_dp = lax.axis_index("dp")
    steps, group_size, top_count = routing.shape
    local_tokens = tokens.shape[1]
    capacity = 2
    old_block = held_weight[0]
    rows, cols = old_block.shape
    row_part = rows // n_dp
    blk = rows // scale_table.shape[1]
    owners = inverse_place(old_expert)
    sources = source_slots(old_expert, new_expert)

    everyone = peers * n_dp
    pieces = old_block.reshape(everyone, rows // everyone, cols)
    staged = lax.all_to_all(pieces, ("ep", "dp"), split_axis=0, concat_axis=0, tiled=True)

    own_scales = scale_table[old_expert[my_slot]]
    col_scales = jnp.repeat(own_scales, blk, axis=1)
    w32 = old_block.reshape(-1, blk, cols).astype(jnp.float32) * col_scales[:, None, :]
    hi32 = lax.reduce_precision(w32, exponent_bits=8, mantissa_bits=7)
    w_hi = hi32.astype(jnp.bfloat16).reshape(rows, cols)
    w_lo = (w32 - hi32).astype(jnp.bfloat16).reshape(rows, cols)
    got = dp_shifts(
        jnp.transpose(tokens.reshape(steps, local_tokens, n_dp, row_part), (2, 0, 1, 3)), n_dp, my_dp
    )
    feats = jnp.stack(got).reshape(n_dp * steps * local_tokens, row_part)

    target = route_targets(routing, owners, peers, capacity)
    token_of = jnp.broadcast_to(
        jnp.arange(group_size, dtype=jnp.int32)[None, :, None], (steps, group_size, top_count)
    ).reshape(steps, -1)
    step_of = jnp.broadcast_to(jnp.arange(steps, dtype=jnp.int32)[:, None], token_of.shape)
    part_of = (my_dp - token_of // local_tokens) % n_dp
    row_of = (part_of * steps + step_of) * local_tokens + token_of % local_tokens
    pick = jnp.zeros((peers * steps * capacity,), jnp.int32).at[target.reshape(-1)].set(row_of.reshape(-1))
    send_tokens = feats[pick].reshape(peers, steps * capacity, row_part)
    staged, send_tokens, w_hi, w_lo = lax.optimization_barrier((staged, send_tokens, w_hi, w_lo))
    arrived = lax.all_to_all(send_tokens, "ep", split_axis=0, concat_axis=0, tiled=True)

    holder = jnp.arange(everyone, dtype=jnp.int32)
    from_block = sources[holder // n_dp] * n_dp + holder % n_dp
    regrouped, arrived = lax.optimization_barrier((jnp.take(staged, from_block, axis=0), arrived))
    new_block = lax.all_to_all(regrouped, ("ep", "dp"), split_axis=0, concat_axis=0, tiled=True).reshape(rows, cols)

    arrived = arrived.reshape(peers * steps * capacity, row_part)
    full = lax.all_gather(arrived, "dp", axis=1, tiled=True)
    hidden = jnp.dot(full, w_hi, preferred_element_type=jnp.float32) + jnp.dot(
        full, w_lo, preferred_element_type=jnp.float32
    )
    act = jax.nn.silu(hidden).astype(jnp.bfloat16)
    act = act.reshape(peers, steps * capacity, cols)
    act, new_block = lax.optimization_barrier((act, new_block))
    returned = lax.all_to_all(act, "ep", split_axis=0, concat_axis=0, tiled=True)
    returned = returned.reshape(peers * steps * capacity, -1)
    picked = returned[target].astype(jnp.float32).reshape(steps, group_size, top_count, -1)
    combined = jnp.sum(gate_values[:, :, :, None] * picked, axis=2).astype(jnp.bfloat16)
    return (combined, new_block[None])


def solution(mesh):
    placed = (
        P(None, ("ep", "dp"), None),
        P(None, "ep", None),
        P(None, "ep", None),
        P("ep", None, "dp"),
        P(None, None, "dp"),
        P(),
        P(),
    )
    return jax.shard_map(
        layer,
        mesh=mesh,
        in_specs=placed,
        out_specs=(P(None, "ep", "dp"), P("ep", None, "dp")),
        check_vma=False,
    )
```

```python
import jax
import jax.numpy as jnp
from jax import lax
from jax.sharding import PartitionSpec as P


def inverse_place(expert_at):
    count = expert_at.shape[0]
    labels = jnp.arange(count, dtype=jnp.int32)
    match = expert_at[None, :] == labels[:, None]
    return jnp.sum(jnp.where(match, labels[None, :], 0), axis=1)


def source_slots(old_expert, new_expert):
    labels = jnp.arange(old_expert.shape[0], dtype=jnp.int32)
    match = old_expert[None, :] == new_expert[:, None]
    return jnp.sum(jnp.where(match, labels[None, :], 0), axis=1)


def route_targets(routing, owners, peers, capacity):
    steps, group_size, top_count = routing.shape
    labels = jnp.arange(peers, dtype=jnp.int32)
    pair_ids = routing.reshape(steps, group_size * top_count)
    onehot = (pair_ids[:, :, None] == labels[None, None, :]).astype(jnp.int32)
    before = jnp.cumsum(onehot, axis=1) - onehot
    rank = jnp.sum(before * onehot, axis=2)
    slot = owners[pair_ids]
    step = jnp.arange(steps, dtype=jnp.int32)[:, None]
    return (slot * steps + step) * capacity + rank


def dp_shifts(parts, n_dp, my_dp):
    got = [parts[my_dp]]
    for shift in range(1, n_dp):
        pairs = [(k, (k + shift) % n_dp) for k in range(n_dp)]
        got.append(lax.ppermute(parts[(my_dp + shift) % n_dp], "dp", pairs))
    return got


def layer(tokens, routing, gate_values, held_weight, scale_table, old_expert, new_expert):
    peers = lax.axis_size("ep")
    n_dp = lax.axis_size("dp")
    my_slot = lax.axis_index("ep")
    my_dp = lax.axis_index("dp")
    steps, group_size, top_count = routing.shape
    local_tokens = tokens.shape[1]
    capacity = 2
    old_block = held_weight[0]
    rows, cols = old_block.shape
    row_part = rows // n_dp
    blk = rows // scale_table.shape[1]
    owners = inverse_place(old_expert)
    sources = source_slots(old_expert, new_expert)

    pieces = old_block.reshape(peers, 2, rows * cols // (2 * peers))
    staged = lax.all_to_all(pieces, "ep", split_axis=0, concat_axis=0, tiled=True)

    own_scales = scale_table[old_expert[my_slot]]
    col_scales = jnp.repeat(own_scales, blk, axis=1)
    w32 = old_block.reshape(-1, blk, cols).astype(jnp.float32) * col_scales[:, None, :]
    hi32 = lax.reduce_precision(w32, exponent_bits=8, mantissa_bits=7)
    w_hi = hi32.astype(jnp.bfloat16).reshape(rows, cols)
    w_lo = (w32 - hi32).astype(jnp.bfloat16).reshape(rows, cols)
    got = dp_shifts(
        jnp.transpose(tokens.reshape(steps, local_tokens, n_dp, row_part), (2, 0, 1, 3)), n_dp, my_dp
    )
    feats = jnp.stack(got).reshape(n_dp * steps * local_tokens, row_part)

    target = route_targets(routing, owners, peers, capacity)
    token_of = jnp.broadcast_to(
        jnp.arange(group_size, dtype=jnp.int32)[None, :, None], (steps, group_size, top_count)
    ).reshape(steps, -1)
    step_of = jnp.broadcast_to(jnp.arange(steps, dtype=jnp.int32)[:, None], token_of.shape)
    part_of = (my_dp - token_of // local_tokens) % n_dp
    row_of = (part_of * steps + step_of) * local_tokens + token_of % local_tokens
    pick = jnp.zeros((peers * steps * capacity,), jnp.int32).at[target.reshape(-1)].set(row_of.reshape(-1))
    send_tokens = feats[pick].reshape(peers, steps * capacity, row_part)
    staged, send_tokens, w_hi, w_lo = lax.optimization_barrier((staged, send_tokens, w_hi, w_lo))
    arrived = lax.all_to_all(send_tokens, "ep", split_axis=0, concat_axis=0, tiled=True)

    regrouped, arrived = lax.optimization_barrier((jnp.take(staged, sources, axis=0), arrived))
    new_block = lax.all_to_all(regrouped, "ep", split_axis=0, concat_axis=0, tiled=True)

    arrived = arrived.reshape(peers * steps * capacity, row_part)
    full = lax.all_gather(arrived, "dp", axis=1, tiled=True)
    hidden = jnp.dot(full, w_hi, preferred_element_type=jnp.float32) + jnp.dot(
        full, w_lo, preferred_element_type=jnp.float32
    )
    act = jax.nn.silu(hidden).astype(jnp.bfloat16)
    act = act.reshape(peers, steps * capacity, cols)
    act, new_block = lax.optimization_barrier((act, new_block))
    returned = lax.all_to_all(act, "ep", split_axis=0, concat_axis=0, tiled=True)
    new_block = new_block.reshape(rows, cols)
    returned = returned.reshape(peers * steps * capacity, -1)
    picked = returned[target].astype(jnp.float32).reshape(steps, group_size, top_count, -1)
    combined = jnp.sum(gate_values[:, :, :, None] * picked, axis=2).astype(jnp.bfloat16)
    return (combined, new_block[None])


def solution(mesh):
    placed = (
        P(None, ("ep", "dp"), None),
        P(None, "ep", None),
        P(None, "ep", None),
        P("ep", None, "dp"),
        P(None, None, "dp"),
        P(),
        P(),
    )
    return jax.shard_map(
        layer,
        mesh=mesh,
        in_specs=placed,
        out_specs=(P(None, "ep", "dp"), P("ep", None, "dp")),
        check_vma=False,
    )
```
